512 devices in a mesh: shot: 32 (over z, y_hi), dom: 16 (over x, y_lo, core).
Axes of the slice: x: 4, y: 8 (y_hi: 4, y_lo: 2; y = y_hi * 2 + y_lo), z: 8, core: 2. Of those that a mesh axis runs over, the one named last changes fastest.
Arguments:
- coefficient: float32 [512, 16, 384], P('dom'), may hold values from 0.02 to 0.18
- fwd_older: float32 [32, 512, 16, 384], P('shot', 'dom'), may hold values from -6 to 6
- fwd_recent: float32 [32, 512, 16, 384], P('shot', 'dom'), may hold values from -6 to 6
- adj_later: float32 [32, 512, 16, 384], P('shot', 'dom'), may hold values from -6 to 6
- adj_recent: float32 [32, 512, 16, 384], P('shot', 'dom'), may hold values from -6 to 6
- source_xcell: int32 [32], P('shot'), may hold values from 0 to 511
- source_ycell: int32 [32], P('shot'), may hold values from 0 to 15
- source_zcell: int32 [32], P('shot'), may hold values from 0 to 383
- amplitude: float32 [32, 2], P('shot'), may hold values from 3547.24 to 7094.48
- receiver_xcell: int32 [32, 1024], P('shot'), may hold values from 0 to 511
- receiver_ycell: int32 [32, 1024], P('shot'), may hold values from 0 to 15
- receiver_zcell: int32 [32, 1024], P('shot'), may hold values from 0 to 383
- observed: float32 [32, 2, 1024], P('shot'), may hold values from -6 to 6
Outputs:
- fwd_latest: float32 [32, 512, 16, 384], P('shot', 'dom')
- adj_latest: float32 [32, 512, 16, 384], P('shot', 'dom')
- model_gradient: float32 [512, 16, 384], P('dom')
The draws below stay inside these ranges and needn't reach their ends.
All inputs are finite; a program needn't handle non-finite values.
Results may differ from the reference program's by a relative error of at most 0.0003.
Values sent between devices are 32-bit elements; how exact they have to be, the bound alone decides.
No kernel may reach another device: no remote copies, remote signals or barrier semaphores. Data moves between devices by JAX's collectives and lax.ppermute only.
A program may use at most 64 MiB of HBM per device.

```python
import math
import jax
import jax.numpy as jnp
from jax import lax

R = 4
NY = 16
NZ = 384
RECV = 1024
NX = 512
SHOTS = 32


def with_ends(drawn, rng, smallest, top_value):
    shape = drawn.shape
    place = [jax.random.randint(jax.random.fold_in(rng, axis), (), 0, shape[axis]) for axis in range(len(shape))]
    drawn = drawn.at[tuple(place)].set(smallest)
    longest = shape.index(max(shape))
    place[longest] = (place[longest] + 1) % shape[longest]
    return drawn.at[tuple(place)].set(top_value)


def level_of(own_key, dims, cuts, smallest, high):
    gain = 1.0
    for position, blocks in cuts:
        steps = jax.random.uniform(jax.random.fold_in(jax.random.fold_in(own_key, 6), position), (blocks,), jnp.float32, smallest / len(cuts), high / len(cuts))
        gain = gain * jnp.repeat(jnp.exp(steps), dims[position] // blocks).reshape((-1,) + (1,) * (len(dims) - 1 - position))
    return gain


def noise(stream_key, shape, spread, limit, pieces=(), kind=jnp.bfloat16):
    level = level_of(stream_key, shape, pieces, -0.22, 0.18) if pieces else 1.0
    result = jax.random.normal(stream_key, shape, jnp.float32) * spread * level
    return jnp.minimum(jnp.maximum(result, -limit), limit).astype(kind)


def setup_inputs(seed: int = 0) -> dict:
    keys = jax.random.split(jax.random.key(seed), 14)
    return {
        "coefficient": jnp.clip(jnp.exp(math.log(0.18) - 2.1972246 * jax.random.uniform(keys[0], (NX, NY, NZ), jnp.float32) ** level_of(keys[0], (NX, NY, NZ), ((0, 16),), -0.2, 0.2)), 0.02, 0.18),
        "fwd_older": noise(keys[1], (SHOTS, NX, NY, NZ), 1.0, 6.0, ((0, 32), (1, 16)), jnp.float32),
        "fwd_recent": noise(keys[2], (SHOTS, NX, NY, NZ), 1.0, 6.0, ((0, 32), (1, 16)), jnp.float32),
        "adj_later": noise(keys[3], (SHOTS, NX, NY, NZ), 1.0, 6.0, ((0, 32), (1, 16)), jnp.float32),
        "adj_recent": noise(keys[4], (SHOTS, NX, NY, NZ), 1.0, 6.0, ((0, 32), (1, 16)), jnp.float32),
        "source_xcell": with_ends(jax.random.randint(keys[5], (SHOTS,), 0, NX), jax.random.fold_in(keys[5], 1), 0, NX - 1).astype(jnp.int32),
        "source_ycell": with_ends(jax.random.randint(keys[6], (SHOTS,), 0, NY), jax.random.fold_in(keys[6], 1), 0, NY - 1).astype(jnp.int32),
        "source_zcell": with_ends(jax.random.randint(keys[7], (SHOTS,), 0, NZ), jax.random.fold_in(keys[7], 1), 0, NZ - 1).astype(jnp.int32),
        "amplitude": jnp.clip(3547.24 + 3547.24 * jax.random.uniform(keys[8], (SHOTS, 2), jnp.float32) ** level_of(keys[8], (SHOTS, 2), ((0, 32),), -0.2, 0.2), 3547.24, 7094.48),
        "receiver_xcell": with_ends(jax.random.randint(keys[9], (SHOTS, RECV), 0, NX), jax.random.fold_in(keys[9], 1), 0, NX - 1).astype(jnp.int32),
        "receiver_ycell": with_ends(jax.random.randint(keys[10], (SHOTS, RECV), 0, NY), jax.random.fold_in(keys[10], 1), 0, NY - 1).astype(jnp.int32),
        "receiver_zcell": with_ends(jax.random.randint(keys[11], (SHOTS, RECV), 0, NZ), jax.random.fold_in(keys[11], 1), 0, NZ - 1).astype(jnp.int32),
        "observed": noise(keys[12], (SHOTS, 2, RECV), 1.0, 6.0, ((0, 32),), jnp.float32),
    }


stencil_weights = (-205.0 / 72.0, 8.0 / 5.0, -1.0 / 5.0, 8.0 / 315.0, -1.0 / 560.0)


def laplace_core(extended):
    count = extended.shape[0] - 2 * R
    center = extended[R:R + count]
    width_y = center.shape[1]
    width_z = center.shape[2]
    total = 3.0 * stencil_weights[0] * center
    padded = jnp.pad(center, ((0, 0), (R, R), (R, R)))
    for offset in range(1, R + 1):
        weight = stencil_weights[offset]
        total = total + weight * (extended[R + offset:R + offset + count] + extended[R - offset:R - offset + count])
        total = total + weight * (padded[:, R + offset:R + offset + width_y, R:R + width_z] + padded[:, R - offset:R - offset + width_y, R:R + width_z])
        total = total + weight * (padded[:, R:R + width_y, R + offset:R + offset + width_z] + padded[:, R:R + width_y, R - offset:R - offset + width_z])
    return total


def point_grid(shape, xcells, ycells, zcells, values, start):
    count = shape[0]
    inside = (xcells >= start) & (xcells < start + count)
    local = jnp.clip(xcells - start, 0, count - 1).astype(jnp.int32)
    kept = jnp.where(inside, values, jnp.zeros_like(values))
    return jnp.zeros(shape, values.dtype).at[local, ycells, zcells].add(kept)


def widen(field):
    return jnp.pad(field, ((R, R), (0, 0), (0, 0)))


def reference(coefficient, fwd_older, fwd_recent, adj_later, adj_recent, source_xcell, source_ycell, source_zcell, amplitude, receiver_xcell, receiver_ycell, receiver_zcell, observed):
    shape = coefficient.shape

    def one_shot(carry, inputs):
        older, recent, later, adj_now, sxc, syc, szc, wavelet, rxc, ryc, rzc, recorded = inputs
        first = point_grid(shape, sxc[None], syc[None], szc[None], wavelet[0][None], 0)
        second = point_grid(shape, sxc[None], syc[None], szc[None], wavelet[1][None], 0)
        fwd_two = 2.0 * recent - older + coefficient * (laplace_core(widen(recent)) + first)
        fwd_three = 2.0 * fwd_two - recent + coefficient * (laplace_core(widen(fwd_two)) + second)
        resid_two = fwd_two[rxc, ryc, rzc] - recorded[0]
        resid_three = fwd_three[rxc, ryc, rzc] - recorded[1]
        adj_two = 2.0 * adj_now - later + coefficient * (laplace_core(widen(adj_now)) + point_grid(shape, rxc, ryc, rzc, resid_three, 0))
        adj_one = 2.0 * adj_two - adj_now + coefficient * (laplace_core(widen(adj_two)) + point_grid(shape, rxc, ryc, rzc, resid_two, 0))
        term = adj_one * (fwd_two - 2.0 * recent + older) + adj_two * (fwd_three - 2.0 * fwd_two + recent)
        return carry + term, (fwd_three, adj_one)

    start = jnp.zeros(shape, coefficient.dtype)
    gradient, outputs = lax.scan(one_shot, start, (fwd_older, fwd_recent, adj_later, adj_recent, source_xcell, source_ycell, source_zcell, amplitude, receiver_xcell, receiver_ycell, receiver_zcell, observed))
    return outputs[0], outputs[1], gradient
```

```python
import jax
import jax.numpy as jnp
from jax import lax
from jax.sharding import PartitionSpec as P

R = 4


stencil_weights = (-205.0 / 72.0, 8.0 / 5.0, -1.0 / 5.0, 8.0 / 315.0, -1.0 / 560.0)


def with_halo(block, sides, width):
    for axis, dim in sides:
        count = lax.axis_size(axis)
        forward = [(i, i + 1) for i in range(count - 1)]
        backward = [(target, source) for source, target in forward]
        low = lax.ppermute(
            lax.slice_in_dim(block, block.shape[dim] - width, None, axis=dim), axis, forward
        )
        high = lax.ppermute(lax.slice_in_dim(block, 0, width, axis=dim), axis, backward)
        block = jnp.concatenate([low, block, high], axis=dim)
    return block


def laplace_core(extended):
    count = extended.shape[0] - 2 * R
    center = extended[R : R + count]
    width_y = center.shape[1]
    width_z = center.shape[2]
    total = 3.0 * stencil_weights[0] * center
    padded = jnp.pad(center, ((0, 0), (R, R), (R, R)))
    for offset in range(1, R + 1):
        weight = stencil_weights[offset]
        total = total + weight * (
            extended[R + offset : R + offset + count] + extended[R - offset : R - offset + count]
        )
        total = total + weight * (
            padded[:, R + offset : R + offset + width_y, R : R + width_z]
            + padded[:, R - offset : R - offset + width_y, R : R + width_z]
        )
        total = total + weight * (
            padded[:, R : R + width_y, R + offset : R + offset + width_z]
            + padded[:, R : R + width_y, R - offset : R - offset + width_z]
        )
    return total


def point_grid(shape, xcells, ycells, zcells, values, start):
    count = shape[0]
    inside = (xcells >= start) & (xcells < start + count)
    local = jnp.clip(xcells - start, 0, count - 1)
    kept = jnp.where(inside, values, jnp.zeros_like(values))
    return jnp.zeros(shape, values.dtype).at[local, ycells, zcells].add(kept)


def sample(field, xcells, ycells, zcells, start):
    count = field.shape[0]
    inside = (xcells >= start) & (xcells < start + count)
    local = jnp.clip(xcells - start, 0, count - 1)
    picked = field[local, ycells, zcells]
    return jnp.where(inside, picked, jnp.zeros_like(picked))


def shot_sum(term):
    count = lax.axis_size("shot")
    pieces = term.reshape((count, term.shape[0] // count) + term.shape[1:])
    mine = jnp.sum(lax.all_to_all(pieces, "shot", 0, 0, tiled=False), axis=0)
    spread = jnp.broadcast_to(mine[None], (count,) + mine.shape)
    return lax.all_to_all(spread, "shot", 0, 0, tiled=False).reshape(term.shape)


def shards(
    coefficient,
    fwd_older,
    fwd_recent,
    adj_later,
    adj_recent,
    source_xcell,
    source_ycell,
    source_zcell,
    amplitude,
    receiver_xcell,
    receiver_ycell,
    receiver_zcell,
    observed,
):
    count = coefficient.shape[0]
    shape = coefficient.shape
    base = lax.axis_index("dom") * count
    older = fwd_older[0]
    recent = fwd_recent[0]
    later = adj_later[0]
    adj_now = adj_recent[0]
    rxc = receiver_xcell[0]
    ryc = receiver_ycell[0]
    rzc = receiver_zcell[0]

    def advance(current, before, sources):
        extended = with_halo(current, (("dom", 0),), R)
        return 2.0 * current - before + coefficient * (laplace_core(extended) + sources)

    fwd_two = advance(
        recent,
        older,
        point_grid(shape, source_xcell, source_ycell, source_zcell, amplitude[0, 0:1], base),
    )
    fwd_three = advance(
        fwd_two,
        recent,
        point_grid(shape, source_xcell, source_ycell, source_zcell, amplitude[0, 1:2], base),
    )
    resid_two = sample(fwd_two, rxc, ryc, rzc, base) - observed[0, 0]
    resid_three = sample(fwd_three, rxc, ryc, rzc, base) - observed[0, 1]
    adj_two = advance(adj_now, later, point_grid(shape, rxc, ryc, rzc, resid_three, base))
    late_term = adj_two * (fwd_three - 2.0 * fwd_two + recent)
    adj_one = advance(adj_two, adj_now, point_grid(shape, rxc, ryc, rzc, resid_two, base))
    early_term = adj_one * (fwd_two - 2.0 * recent + older)
    gradient = shot_sum(early_term + late_term)
    return (fwd_three[None], adj_one[None], gradient)


def solution(mesh):
    return jax.shard_map(
        shards,
        mesh=mesh,
        in_specs=(
            P("dom", None, None),
            P("shot", "dom", None, None),
            P("shot", "dom", None, None),
            P("shot", "dom", None, None),
            P("shot", "dom", None, None),
            P("shot"),
            P("shot"),
            P("shot"),
            P("shot", None),
            P("shot", None),
            P("shot", None),
            P("shot", None),
            P("shot", None, None),
        ),
        out_specs=(
            P("shot", "dom", None, None),
            P("shot", "dom", None, None),
            P("dom", None, None),
        ),
        check_vma=False,
    )
```

```python
import jax
import jax.numpy as jnp
from jax import lax
from jax.sharding import PartitionSpec as P

R = 4


stencil_weights = (-205.0 / 72.0, 8.0 / 5.0, -1.0 / 5.0, 8.0 / 315.0, -1.0 / 560.0)


def with_halo(block, sides, width):
    for axis, dim in sides:
        count = lax.axis_size(axis)
        forward = [(i, i + 1) for i in range(count - 1)]
        backward = [(target, source) for source, target in forward]
        low = lax.ppermute(
            lax.slice_in_dim(block, block.shape[dim] - width, None, axis=dim), axis, forward
        )
        high = lax.ppermute(lax.slice_in_dim(block, 0, width, axis=dim), axis, backward)
        block = jnp.concatenate([low, block, high], axis=dim)
    return block


def laplace_core(extended):
    count = extended.shape[0] - 2 * R
    center = extended[R : R + count]
    width_y = center.shape[1]
    width_z = center.shape[2]
    total = 3.0 * stencil_weights[0] * center
    padded = jnp.pad(center, ((0, 0), (R, R), (R, R)))
    for offset in range(1, R + 1):
        weight = stencil_weights[offset]
        total = total + weight * (
            extended[R + offset : R + offset + count] + extended[R - offset : R - offset + count]
        )
        total = total + weight * (
            padded[:, R + offset : R + offset + width_y, R : R + width_z]
            + padded[:, R - offset : R - offset + width_y, R : R + width_z]
        )
        total = total + weight * (
            padded[:, R : R + width_y, R + offset : R + offset + width_z]
            + padded[:, R : R + width_y, R - offset : R - offset + width_z]
        )
    return total


def point_grid(shape, xcells, ycells, zcells, values, start):
    count = shape[0]
    inside = (xcells >= start) & (xcells < start + count)
    local = jnp.clip(xcells - start, 0, count - 1)
    kept = jnp.where(inside, values, jnp.zeros_like(values))
    return jnp.zeros(shape, values.dtype).at[local, ycells, zcells].add(kept)


def selectors(shape, xcells, ycells, zcells, start):
    width_x, width_y, width_z = shape
    inside = (xcells >= start) & (xcells < start + width_x)
    row = jnp.where(inside, (xcells - start) * width_y + ycells, -1)
    count = xcells.shape[0]
    rows = (row[:, None] == lax.broadcasted_iota(jnp.int32, (count, width_x * width_y), 1)).astype(jnp.float32)
    cols = (zcells[:, None] == lax.broadcasted_iota(jnp.int32, (count, width_z), 1)).astype(jnp.float32)
    return rows, cols


def sample(field, rows, cols):
    width_x, width_y, width_z = field.shape
    picked = jnp.dot(rows, field.reshape(width_x * width_y, width_z), precision=lax.Precision.HIGHEST)
    return jnp.sum(picked * cols, axis=1)


def receiver_grid(shape, rows, cols, values):
    placed = lax.dot_general(
        rows * values[:, None], cols, (((0,), (0,)), ((), ())), precision=lax.Precision.HIGHEST
    )
    return placed.reshape(shape)


def shot_sum(term):
    count = lax.axis_size("shot")
    pieces = term.reshape((count, term.shape[0] // count) + term.shape[1:])
    mine = jnp.sum(lax.all_to_all(pieces, "shot", 0, 0, tiled=False), axis=0)
    spread = jnp.broadcast_to(mine[None], (count,) + mine.shape)
    return lax.all_to_all(spread, "shot", 0, 0, tiled=False).reshape(term.shape)


def shards(
    coefficient,
    fwd_older,
    fwd_recent,
    adj_later,
    adj_recent,
    source_xcell,
    source_ycell,
    source_zcell,
    amplitude,
    receiver_xcell,
    receiver_ycell,
    receiver_zcell,
    observed,
):
    count = coefficient.shape[0]
    shape = coefficient.shape
    base = lax.axis_index("dom") * count
    older = fwd_older[0]
    recent = fwd_recent[0]
    later = adj_later[0]
    adj_now = adj_recent[0]
    rxc = receiver_xcell[0]
    ryc = receiver_ycell[0]
    rzc = receiver_zcell[0]

    def advance(current, before, sources):
        extended = with_halo(current, (("dom", 0),), R)
        return 2.0 * current - before + coefficient * (laplace_core(extended) + sources)

    fwd_two = advance(
        recent,
        older,
        point_grid(shape, source_xcell, source_ycell, source_zcell, amplitude[0, 0:1], base),
    )
    fwd_three = advance(
        fwd_two,
        recent,
        point_grid(shape, source_xcell, source_ycell, source_zcell, amplitude[0, 1:2], base),
    )
    rows, cols = selectors(shape, rxc, ryc, rzc, base)
    resid_two = sample(fwd_two, rows, cols) - observed[0, 0]
    resid_three = sample(fwd_three, rows, cols) - observed[0, 1]
    adj_two = advance(adj_now, later, receiver_grid(shape, rows, cols, resid_three))
    late_term = adj_two * (fwd_three - 2.0 * fwd_two + recent)
    adj_one = advance(adj_two, adj_now, receiver_grid(shape, rows, cols, resid_two))
    early_term = adj_one * (fwd_two - 2.0 * recent + older)
    gradient = shot_sum(early_term + late_term)
    return (fwd_three[None], adj_one[None], gradient)


def solution(mesh):
    return jax.shard_map(
        shards,
        mesh=mesh,
        in_specs=(
            P("dom", None, None),
            P("shot", "dom", None, None),
            P("shot", "dom", None, None),
            P("shot", "dom", None, None),
            P("shot", "dom", None, None),
            P("shot"),
            P("shot"),
            P("shot"),
            P("shot", None),
            P("shot", None),
            P("shot", None),
            P("shot", None),
            P("shot", None, None),
        ),
        out_specs=(
            P("shot", "dom", None, None),
            P("shot", "dom", None, None),
            P("dom", None, None),
        ),
        check_vma=False,
    )
```

```python
import jax
import jax.numpy as jnp
from jax import lax
from jax.sharding import PartitionSpec as P

R = 4


stencil_weights = (-205.0 / 72.0, 8.0 / 5.0, -1.0 / 5.0, 8.0 / 315.0, -1.0 / 560.0)


def with_halo(block, sides, width):
    for axis, dim in sides:
        count = lax.axis_size(axis)
        forward = [(i, i + 1) for i in range(count - 1)]
        backward = [(target, source) for source, target in forward]
        low = lax.ppermute(
            lax.slice_in_dim(block, block.shape[dim] - width, None, axis=dim), axis, forward
        )
        high = lax.ppermute(lax.slice_in_dim(block, 0, width, axis=dim), axis, backward)
        block = jnp.concatenate([low, block, high], axis=dim)
    return block


def wide_halo(fields, widths):
    count = lax.axis_size("dom")
    forward = [(i, i + 1) for i in range(count - 1)]
    backward = [(target, source) for source, target in forward]
    tails = jnp.concatenate([f[f.shape[0] - w :] for f, w in zip(fields, widths)])
    heads = jnp.concatenate([f[:w] for f, w in zip(fields, widths)])
    lows = lax.ppermute(tails, "dom", forward)
    highs = lax.ppermute(heads, "dom", backward)
    out, at = [], 0
    for f, w in zip(fields, widths):
        out.append(jnp.concatenate([lows[at : at + w], f, highs[at : at + w]]))
        at += w
    return out


def laplace_core(extended):
    count = extended.shape[0] - 2 * R
    center = extended[R : R + count]
    width_y = center.shape[1]
    width_z = center.shape[2]
    total = 3.0 * stencil_weights[0] * center
    padded = jnp.pad(center, ((0, 0), (R, R), (R, R)))
    for offset in range(1, R + 1):
        weight = stencil_weights[offset]
        total = total + weight * (
            extended[R + offset : R + offset + count] + extended[R - offset : R - offset + count]
        )
        total = total + weight * (
            padded[:, R + offset : R + offset + width_y, R : R + width_z]
            + padded[:, R - offset : R - offset + width_y, R : R + width_z]
        )
        total = total + weight * (
            padded[:, R : R + width_y, R + offset : R + offset + width_z]
            + padded[:, R : R + width_y, R - offset : R - offset + width_z]
        )
    return total


def point_grid(shape, xcells, ycells, zcells, values, start):
    count = shape[0]
    inside = (xcells >= start) & (xcells < start + count)
    local = jnp.clip(xcells - start, 0, count - 1)
    kept = jnp.where(inside, values, jnp.zeros_like(values))
    return jnp.zeros(shape, values.dtype).at[local, ycells, zcells].add(kept)


def selectors(shape, xcells, ycells, zcells, start):
    width_x, width_y, width_z = shape
    inside = (xcells >= start) & (xcells < start + width_x)
    row = jnp.where(inside, (xcells - start) * width_y + ycells, -1)
    count = xcells.shape[0]
    rows = (row[:, None] == lax.broadcasted_iota(jnp.int32, (count, width_x * width_y), 1)).astype(jnp.float32)
    cols = (zcells[:, None] == lax.broadcasted_iota(jnp.int32, (count, width_z), 1)).astype(jnp.float32)
    return rows, cols


def sample(field, rows, cols):
    width_x, width_y, width_z = field.shape
    picked = jnp.dot(rows, field.reshape(width_x * width_y, width_z), precision=lax.Precision.HIGHEST)
    return jnp.sum(picked * cols, axis=1)


def receiver_grid(shape, rows, cols, values):
    placed = lax.dot_general(
        rows * values[:, None], cols, (((0,), (0,)), ((), ())), precision=lax.Precision.HIGHEST
    )
    return placed.reshape(shape)


def shot_sum(term):
    count = lax.axis_size("shot")
    pieces = term.reshape((count, term.shape[0] // count) + term.shape[1:])
    mine = jnp.sum(lax.all_to_all(pieces, "shot", 0, 0, tiled=False), axis=0)
    spread = jnp.broadcast_to(mine[None], (count,) + mine.shape)
    return lax.all_to_all(spread, "shot", 0, 0, tiled=False).reshape(term.shape)


def shards(
    coefficient,
    fwd_older,
    fwd_recent,
    adj_later,
    adj_recent,
    source_xcell,
    source_ycell,
    source_zcell,
    amplitude,
    receiver_xcell,
    receiver_ycell,
    receiver_zcell,
    observed,
):
    count = coefficient.shape[0]
    shape = coefficient.shape
    base = lax.axis_index("dom") * count
    older = fwd_older[0]
    recent = fwd_recent[0]
    later = adj_later[0]
    adj_now = adj_recent[0]
    rxc = receiver_xcell[0]
    ryc = receiver_ycell[0]
    rzc = receiver_zcell[0]

    widths = (3 * R, 2 * R, 2 * R, 2 * R, R)
    fields = (recent, older, coefficient, adj_now, later)
    recent_x, older_x, coef_x, adj_now_x, later_x = wide_halo(fields, widths)

    def advance(current, before, coef, sources):
        return 2.0 * current[R:-R] - before + coef * (laplace_core(current) + sources)

    def region(margin):
        return (count + 2 * margin,) + shape[1:]

    def source_grid(margin, step):
        return point_grid(
            region(margin), source_xcell, source_ycell, source_zcell,
            amplitude[0, step : step + 1], base - margin,
        )

    fwd_two_x = advance(recent_x, older_x, coef_x, source_grid(2 * R, 0))
    fwd_three_x = advance(fwd_two_x, recent_x[2 * R : -2 * R], coef_x[R:-R], source_grid(R, 1))
    rows_x, cols = selectors(region(R), rxc, ryc, rzc, base - R)
    rows = rows_x[:, R * shape[1] : (R + count) * shape[1]]
    fwd_two = fwd_two_x[2 * R : -2 * R]
    fwd_three = fwd_three_x[R:-R]
    resid_two = sample(fwd_two, rows, cols) - observed[0, 0]
    resid_three = sample(fwd_three_x, rows_x, cols) - observed[0, 1]
    adj_two_x = advance(
        adj_now_x, later_x, coef_x[R:-R], receiver_grid(region(R), rows_x, cols, resid_three)
    )
    adj_one = advance(
        adj_two_x, adj_now_x[2 * R : -2 * R], coefficient, receiver_grid(shape, rows, cols, resid_two)
    )
    adj_two = adj_two_x[R:-R]
    recent_own = recent_x[3 * R : -3 * R]
    late_term = adj_two * (fwd_three - 2.0 * fwd_two + recent_own)
    early_term = adj_one * (fwd_two - 2.0 * recent_own + older)
    gradient = shot_sum(early_term + late_term)
    return (fwd_three[None], adj_one[None], gradient)


def solution(mesh):
    return jax.shard_map(
        shards,
        mesh=mesh,
        in_specs=(
            P("dom", None, None),
            P("shot", "dom", None, None),
            P("shot", "dom", None, None),
            P("shot", "dom", None, None),
            P("shot", "dom", None, None),
            P("shot"),
            P("shot"),
            P("shot"),
            P("shot", None),
            P("shot", None),
            P("shot", None),
            P("shot", None),
            P("shot", None, None),
        ),
        out_specs=(
            P("shot", "dom", None, None),
            P("shot", "dom", None, None),
            P("dom", None, None),
        ),
        check_vma=False,
    )
```

```python
import jax
import jax.numpy as jnp
from jax import lax
from jax.sharding import PartitionSpec as P

R = 4


stencil_weights = (-205.0 / 72.0, 8.0 / 5.0, -1.0 / 5.0, 8.0 / 315.0, -1.0 / 560.0)


def with_halo(block, sides, width):
    for axis, dim in sides:
        count = lax.axis_size(axis)
        forward = [(i, i + 1) for i in range(count - 1)]
        backward = [(target, source) for source, target in forward]
        low = lax.ppermute(
            lax.slice_in_dim(block, block.shape[dim] - width, None, axis=dim), axis, forward
        )
        high = lax.ppermute(lax.slice_in_dim(block, 0, width, axis=dim), axis, backward)
        block = jnp.concatenate([low, block, high], axis=dim)
    return block


def wide_halo(fields, widths):
    count = lax.axis_size("dom")
    forward = [(i, i + 1) for i in range(count - 1)]
    backward = [(target, source) for source, target in forward]
    tails = jnp.concatenate([f[f.shape[0] - w :] for f, w in zip(fields, widths)])
    heads = jnp.concatenate([f[:w] for f, w in zip(fields, widths)])
    lows = lax.ppermute(tails, "dom", forward)
    highs = lax.ppermute(heads, "dom", backward)
    out, at = [], 0
    for f, w in zip(fields, widths):
        out.append(jnp.concatenate([lows[at : at + w], f, highs[at : at + w]]))
        at += w
    return out


def laplace_core(extended):
    count = extended.shape[0] - 2 * R
    center = extended[R : R + count]
    width_y = center.shape[1]
    width_z = center.shape[2]
    total = 3.0 * stencil_weights[0] * center
    padded = jnp.pad(center, ((0, 0), (R, R), (R, R)))
    for offset in range(1, R + 1):
        weight = stencil_weights[offset]
        total = total + weight * (
            extended[R + offset : R + offset + count] + extended[R - offset : R - offset + count]
        )
        total = total + weight * (
            padded[:, R + offset : R + offset + width_y, R : R + width_z]
            + padded[:, R - offset : R - offset + width_y, R : R + width_z]
        )
        total = total + weight * (
            padded[:, R : R + width_y, R + offset : R + offset + width_z]
            + padded[:, R : R + width_y, R - offset : R - offset + width_z]
        )
    return total


def point_grid(shape, xcells, ycells, zcells, values, start):
    count = shape[0]
    inside = (xcells >= start) & (xcells < start + count)
    local = jnp.clip(xcells - start, 0, count - 1)
    kept = jnp.where(inside, values, jnp.zeros_like(values))
    return jnp.zeros(shape, values.dtype).at[local, ycells, zcells].add(kept)


def selectors(shape, xcells, ycells, zcells, start):
    width_x, width_y, width_z = shape
    inside = (xcells >= start) & (xcells < start + width_x)
    row = jnp.where(inside, (xcells - start) * width_y + ycells, -1)
    count = xcells.shape[0]
    rows = (row[:, None] == lax.broadcasted_iota(jnp.int32, (count, width_x * width_y), 1)).astype(jnp.float32)
    cols = (zcells[:, None] == lax.broadcasted_iota(jnp.int32, (count, width_z), 1)).astype(jnp.float32)
    return rows, cols


def sample(field, rows, cols):
    width_x, width_y, width_z = field.shape
    picked = jnp.dot(rows, field.reshape(width_x * width_y, width_z), precision=lax.Precision.HIGHEST)
    return jnp.sum(picked * cols, axis=1)


def receiver_grid(shape, rows, cols, values):
    placed = lax.dot_general(
        rows * values[:, None], cols, (((0,), (0,)), ((), ())), precision=lax.Precision.HIGHEST
    )
    return placed.reshape(shape)


def shot_sum(term):
    count = lax.axis_size("shot")
    pieces = term.reshape((count, term.shape[0] // count) + term.shape[1:])
    mine = jnp.sum(lax.all_to_all(pieces, "shot", 0, 0, tiled=False), axis=0)
    spread = jnp.broadcast_to(mine[None], (count,) + mine.shape)
    return lax.all_to_all(spread, "shot", 0, 0, tiled=False).reshape(term.shape)


def shards(
    coefficient,
    fwd_older,
    fwd_recent,
    adj_later,
    adj_recent,
    source_xcell,
    source_ycell,
    source_zcell,
    amplitude,
    receiver_xcell,
    receiver_ycell,
    receiver_zcell,
    observed,
):
    count = coefficient.shape[0]
    shape = coefficient.shape
    base = lax.axis_index("dom") * count
    older = fwd_older[0]
    recent = fwd_recent[0]
    later = adj_later[0]
    adj_now = adj_recent[0]
    rxc = receiver_xcell[0]
    ryc = receiver_ycell[0]
    rzc = receiver_zcell[0]

    widths = (2 * R, R, R, R)
    fields = (recent, older, coefficient, adj_now)
    recent_x, older_x, coef_x, adj_now_x = wide_halo(fields, widths)

    def advance(current, before, coef, sources):
        return 2.0 * current[R:-R] - before + coef * (laplace_core(current) + sources)

    def source_grid(margin, step):
        return point_grid(
            (count + 2 * margin,) + shape[1:], source_xcell, source_ycell, source_zcell,
            amplitude[0, step : step + 1], base - margin,
        )

    fwd_two_x = advance(recent_x, older_x, coef_x, source_grid(R, 0))
    fwd_two = fwd_two_x[R:-R]
    recent_own = recent_x[2 * R : -2 * R]
    fwd_three = advance(fwd_two_x, recent_own, coefficient, source_grid(0, 1))
    rows, cols = selectors(shape, rxc, ryc, rzc, base)
    resid_two = sample(fwd_two, rows, cols) - observed[0, 0]
    resid_three = sample(fwd_three, rows, cols) - observed[0, 1]
    adj_two = advance(adj_now_x, later, coefficient, receiver_grid(shape, rows, cols, resid_three))
    adj_one = advance(
        with_halo(adj_two, (("dom", 0),), R), adj_now, coefficient,
        receiver_grid(shape, rows, cols, resid_two),
    )
    late_term = adj_two * (fwd_three - 2.0 * fwd_two + recent_own)
    early_term = adj_one * (fwd_two - 2.0 * recent_own + older)
    gradient = shot_sum(early_term + late_term)
    return (fwd_three[None], adj_one[None], gradient)


def solution(mesh):
    return jax.shard_map(
        shards,
        mesh=mesh,
        in_specs=(
            P("dom", None, None),
            P("shot", "dom", None, None),
            P("shot", "dom", None, None),
            P("shot", "dom", None, None),
            P("shot", "dom", None, None),
            P("shot"),
            P("shot"),
            P("shot"),
            P("shot", None),
            P("shot", None),
            P("shot", None),
            P("shot", None),
            P("shot", None, None),
        ),
        out_specs=(
            P("shot", "dom", None, None),
            P("shot", "dom", None, None),
            P("dom", None, None),
        ),
        check_vma=False,
    )
```

```python
import jax
import jax.numpy as jnp
from jax import lax
from jax.sharding import PartitionSpec as P

R = 4


stencil_weights = (-205.0 / 72.0, 8.0 / 5.0, -1.0 / 5.0, 8.0 / 315.0, -1.0 / 560.0)


def with_halo(block, sides, width):
    for axis, dim in sides:
        count = lax.axis_size(axis)
        forward = [(i, i + 1) for i in range(count - 1)]
        backward = [(target, source) for source, target in forward]
        low = lax.ppermute(
            lax.slice_in_dim(block, block.shape[dim] - width, None, axis=dim), axis, forward
        )
        high = lax.ppermute(lax.slice_in_dim(block, 0, width, axis=dim), axis, backward)
        block = jnp.concatenate([low, block, high], axis=dim)
    return block


def window(field, start, stop):
    low, own, high = field
    count = own.shape[0]
    parts = []
    if start < 0:
        parts.append(low[low.shape[0] + start : low.shape[0] + min(stop, 0)])
    if stop > 0 and start < count:
        parts.append(own[max(start, 0) : min(stop, count)])
    if stop > count:
        parts.append(high[max(start - count, 0) : stop - count])
    return parts[0] if len(parts) == 1 else jnp.concatenate(parts)


def with_halo_parts(block, width):
    count = lax.axis_size("dom")
    forward = [(i, i + 1) for i in range(count - 1)]
    backward = [(target, source) for source, target in forward]
    low = lax.ppermute(block[block.shape[0] - width :], "dom", forward)
    high = lax.ppermute(block[:width], "dom", backward)
    return low, high


def wide_halo(fields, widths):
    count = lax.axis_size("dom")
    forward = [(i, i + 1) for i in range(count - 1)]
    backward = [(target, source) for source, target in forward]
    tails = jnp.concatenate([f[f.shape[0] - w :] for f, w in zip(fields, widths)])
    heads = jnp.concatenate([f[:w] for f, w in zip(fields, widths)])
    lows = lax.ppermute(tails, "dom", forward)
    highs = lax.ppermute(heads, "dom", backward)
    out, at = [], 0
    for w in widths:
        out.append((lows[at : at + w], highs[at : at + w]))
        at += w
    return out


def laplace_core(extended):
    count = extended.shape[0] - 2 * R
    center = extended[R : R + count]
    width_y = center.shape[1]
    width_z = center.shape[2]
    total = 3.0 * stencil_weights[0] * center
    padded = jnp.pad(center, ((0, 0), (R, R), (R, R)))
    for offset in range(1, R + 1):
        weight = stencil_weights[offset]
        total = total + weight * (
            extended[R + offset : R + offset + count] + extended[R - offset : R - offset + count]
        )
        total = total + weight * (
            padded[:, R + offset : R + offset + width_y, R : R + width_z]
            + padded[:, R - offset : R - offset + width_y, R : R + width_z]
        )
        total = total + weight * (
            padded[:, R : R + width_y, R + offset : R + offset + width_z]
            + padded[:, R : R + width_y, R - offset : R - offset + width_z]
        )
    return total


def point_grid(shape, xcells, ycells, zcells, values, start):
    count = shape[0]
    inside = (xcells >= start) & (xcells < start + count)
    local = jnp.clip(xcells - start, 0, count - 1)
    kept = jnp.where(inside, values, jnp.zeros_like(values))
    return jnp.zeros(shape, values.dtype).at[local, ycells, zcells].add(kept)


def selectors(shape, xcells, ycells, zcells, start):
    width_x, width_y, width_z = shape
    inside = (xcells >= start) & (xcells < start + width_x)
    row = jnp.where(inside, (xcells - start) * width_y + ycells, -1)
    count = xcells.shape[0]
    rows = (row[:, None] == lax.broadcasted_iota(jnp.int32, (count, width_x * width_y), 1)).astype(jnp.float32)
    cols = (zcells[:, None] == lax.broadcasted_iota(jnp.int32, (count, width_z), 1)).astype(jnp.float32)
    return rows, cols


def sample(field, rows, cols):
    width_x, width_y, width_z = field.shape
    picked = jnp.dot(rows, field.reshape(width_x * width_y, width_z), precision=lax.Precision.HIGHEST)
    return jnp.sum(picked * cols, axis=1)


def receiver_grid(shape, rows, cols, values):
    placed = lax.dot_general(
        rows * values[:, None], cols, (((0,), (0,)), ((), ())), precision=lax.Precision.HIGHEST
    )
    return placed.reshape(shape)


def shot_sum(term):
    count = lax.axis_size("shot")
    pieces = term.reshape((count, term.shape[0] // count) + term.shape[1:])
    mine = jnp.sum(lax.all_to_all(pieces, "shot", 0, 0, tiled=False), axis=0)
    spread = jnp.broadcast_to(mine[None], (count,) + mine.shape)
    return lax.all_to_all(spread, "shot", 0, 0, tiled=False).reshape(term.shape)


def shards(
    coefficient,
    fwd_older,
    fwd_recent,
    adj_later,
    adj_recent,
    source_xcell,
    source_ycell,
    source_zcell,
    amplitude,
    receiver_xcell,
    receiver_ycell,
    receiver_zcell,
    observed,
):
    count = coefficient.shape[0]
    shape = coefficient.shape
    base = lax.axis_index("dom") * count
    older = fwd_older[0]
    recent = fwd_recent[0]
    later = adj_later[0]
    adj_now = adj_recent[0]
    rxc = receiver_xcell[0]
    ryc = receiver_ycell[0]
    rzc = receiver_zcell[0]

    widths = (2 * R, R, R, R)
    fields = (recent, older, coefficient, adj_now)
    halos = wide_halo(fields, widths)
    recent_t, older_t, coef_t, adj_now_t = [(lo, f, hi) for f, (lo, hi) in zip(fields, halos)]
    later_t = (None, later, None)
    inner = [(-R, R), (R, count - R), (count - R, count + R)]
    split = [(0, R), (R, count - R), (count - R, count)]

    def source_grid(step, margin):
        grid = point_grid(
            (count + 2 * margin,) + shape[1:], source_xcell, source_ycell, source_zcell,
            amplitude[0, step : step + 1], base - margin,
        )
        return lambda a, b: grid[a + margin : b + margin]

    def laplace_parts(current, pieces):
        return [laplace_core(window(current, a - R, b + R)) for a, b in pieces]

    def advance(current, before, laplace, sources, pieces):
        return [
            2.0 * window(current, a, b) - window(before, a, b)
            + window(coef_t, a, b) * (lap + sources(a, b))
            for lap, (a, b) in zip(laplace, pieces)
        ]

    fwd_two_p = advance(
        recent_t, older_t, laplace_parts(recent_t, inner), source_grid(0, R), inner
    )
    fwd_two_t = (
        fwd_two_p[0][:R],
        jnp.concatenate([fwd_two_p[0][R:], fwd_two_p[1], fwd_two_p[2][:R]]),
        fwd_two_p[2][R:],
    )
    fwd_two = fwd_two_t[1]
    (fwd_three,) = advance(
        fwd_two_t, recent_t, laplace_parts(fwd_two_t, [(0, count)]), source_grid(1, 0), [(0, count)]
    )
    rows, cols = selectors(shape, rxc, ryc, rzc, base)
    resid_two = sample(fwd_two, rows, cols) - observed[0, 0]
    resid_three = sample(fwd_three, rows, cols) - observed[0, 1]
    adj_lap = lax.optimization_barrier(laplace_parts(adj_now_t, split))
    adj_sources = receiver_grid(shape, rows, cols, resid_three)
    adj_two_p = advance(
        adj_now_t, later_t, adj_lap, lambda a, b: adj_sources[a:b], split
    )
    adj_two = jnp.concatenate(adj_two_p)
    adj_two_low, adj_two_high = with_halo_parts(adj_two, R)
    adj_two_t = (adj_two_low, adj_two, adj_two_high)
    adj_sources_two = receiver_grid(shape, rows, cols, resid_two)
    adj_one_p = advance(
        adj_two_t, adj_now_t, laplace_parts(adj_two_t, split),
        lambda a, b: adj_sources_two[a:b], split,
    )
    adj_one = jnp.concatenate(adj_one_p)
    terms = []
    for one, (a, b) in zip(adj_one_p, split):
        recent_ab = recent[a:b]
        terms.append(
            one * (fwd_two[a:b] - 2.0 * recent_ab + older[a:b])
            + adj_two[a:b] * (fwd_three[a:b] - 2.0 * fwd_two[a:b] + recent_ab)
        )
    gradient = shot_sum(jnp.concatenate(terms))
    return (fwd_three[None], adj_one[None], gradient)


def solution(mesh):
    return jax.shard_map(
        shards,
        mesh=mesh,
        in_specs=(
            P("dom", None, None),
            P("shot", "dom", None, None),
            P("shot", "dom", None, None),
            P("shot", "dom", None, None),
            P("shot", "dom", None, None),
            P("shot"),
            P("shot"),
            P("shot"),
            P("shot", None),
            P("shot", None),
            P("shot", None),
            P("shot", None),
            P("shot", None, None),
        ),
        out_specs=(
            P("shot", "dom", None, None),
            P("shot", "dom", None, None),
            P("dom", None, None),
        ),
        check_vma=False,
    )
```

```python
import jax
import jax.numpy as jnp
from jax import lax
from jax.sharding import PartitionSpec as P

R = 4


stencil_weights = (-205.0 / 72.0, 8.0 / 5.0, -1.0 / 5.0, 8.0 / 315.0, -1.0 / 560.0)


def with_halo(block, sides, width):
    for axis, dim in sides:
        count = lax.axis_size(axis)
        forward = [(i, i + 1) for i in range(count - 1)]
        backward = [(target, source) for source, target in forward]
        low = lax.ppermute(
            lax.slice_in_dim(block, block.shape[dim] - width, None, axis=dim), axis, forward
        )
        high = lax.ppermute(lax.slice_in_dim(block, 0, width, axis=dim), axis, backward)
        block = jnp.concatenate([low, block, high], axis=dim)
    return block


def wide_halo(fields, widths):
    count = lax.axis_size("dom")
    forward = [(i, i + 1) for i in range(count - 1)]
    backward = [(target, source) for source, target in forward]
    tails = jnp.concatenate([f[f.shape[0] - w :] for f, w in zip(fields, widths)])
    heads = jnp.concatenate([f[:w] for f, w in zip(fields, widths)])
    lows = lax.ppermute(tails, "dom", forward)
    highs = lax.ppermute(heads, "dom", backward)
    out, at = [], 0
    for f, w in zip(fields, widths):
        out.append(jnp.concatenate([lows[at : at + w], f, highs[at : at + w]]))
        at += w
    return out


def laplace_core(extended):
    count = extended.shape[0] - 2 * R
    center = extended[R : R + count]
    width_y = center.shape[1]
    width_z = center.shape[2]
    total = 3.0 * stencil_weights[0] * center
    padded = jnp.pad(center, ((0, 0), (R, R), (R, R)))
    for offset in range(1, R + 1):
        weight = stencil_weights[offset]
        total = total + weight * (
            extended[R + offset : R + offset + count] + extended[R - offset : R - offset + count]
        )
        total = total + weight * (
            padded[:, R + offset : R + offset + width_y, R : R + width_z]
            + padded[:, R - offset : R - offset + width_y, R : R + width_z]
        )
        total = total + weight * (
            padded[:, R : R + width_y, R + offset : R + offset + width_z]
            + padded[:, R : R + width_y, R - offset : R - offset + width_z]
        )
    return total


def point_grid(shape, xcells, ycells, zcells, values, start):
    count = shape[0]
    inside = (xcells >= start) & (xcells < start + count)
    local = jnp.clip(xcells - start, 0, count - 1)
    kept = jnp.where(inside, values, jnp.zeros_like(values))
    return jnp.zeros(shape, values.dtype).at[local, ycells, zcells].add(kept)


def selectors(shape, xcells, ycells, zcells, start):
    width_x, width_y, width_z = shape
    inside = (xcells >= start) & (xcells < start + width_x)
    row = jnp.where(inside, (xcells - start) * width_y + ycells, -1)
    count = xcells.shape[0]
    rows = (row[:, None] == lax.broadcasted_iota(jnp.int32, (count, width_x * width_y), 1)).astype(jnp.float32)
    cols = (zcells[:, None] == lax.broadcasted_iota(jnp.int32, (count, width_z), 1)).astype(jnp.float32)
    return rows, cols


def sample(field, rows, cols):
    width_x, width_y, width_z = field.shape
    picked = jnp.dot(rows, field.reshape(width_x * width_y, width_z), precision=lax.Precision.HIGH)
    return jnp.sum(picked * cols, axis=1)


def receiver_grid(shape, rows, cols, values):
    placed = lax.dot_general(
        rows * values[:, None], cols, (((0,), (0,)), ((), ())), precision=lax.Precision.HIGH
    )
    return placed.reshape(shape)


def shot_sum(term):
    count = lax.axis_size("shot")
    pieces = term.reshape((count, term.shape[0] // count) + term.shape[1:])
    mine = jnp.sum(lax.all_to_all(pieces, "shot", 0, 0, tiled=False), axis=0)
    spread = jnp.broadcast_to(mine[None], (count,) + mine.shape)
    return lax.all_to_all(spread, "shot", 0, 0, tiled=False).reshape(term.shape)


def shards(
    coefficient,
    fwd_older,
    fwd_recent,
    adj_later,
    adj_recent,
    source_xcell,
    source_ycell,
    source_zcell,
    amplitude,
    receiver_xcell,
    receiver_ycell,
    receiver_zcell,
    observed,
):
    count = coefficient.shape[0]
    shape = coefficient.shape
    base = lax.axis_index("dom") * count
    older = fwd_older[0]
    recent = fwd_recent[0]
    later = adj_later[0]
    adj_now = adj_recent[0]
    rxc = receiver_xcell[0]
    ryc = receiver_ycell[0]
    rzc = receiver_zcell[0]

    widths = (2 * R, R, R, R)
    fields = (recent, older, coefficient, adj_now)
    recent_x, older_x, coef_x, adj_now_x = wide_halo(fields, widths)

    def advance(current, before, coef, sources):
        return 2.0 * current[R:-R] - before + coef * (laplace_core(current) + sources)

    def source_grid(margin, step):
        return point_grid(
            (count + 2 * margin,) + shape[1:], source_xcell, source_ycell, source_zcell,
            amplitude[0, step : step + 1], base - margin,
        )

    fwd_two_x = advance(recent_x, older_x, coef_x, source_grid(R, 0))
    fwd_two = fwd_two_x[R:-R]
    recent_own = recent_x[2 * R : -2 * R]
    fwd_three = advance(fwd_two_x, recent_own, coefficient, source_grid(0, 1))
    rows, cols = selectors(shape, rxc, ryc, rzc, base)
    resid_two = sample(fwd_two, rows, cols) - observed[0, 0]
    resid_three = sample(fwd_three, rows, cols) - observed[0, 1]
    adj_two = advance(adj_now_x, later, coefficient, receiver_grid(shape, rows, cols, resid_three))
    adj_one = advance(
        with_halo(adj_two, (("dom", 0),), R), adj_now, coefficient,
        receiver_grid(shape, rows, cols, resid_two),
    )
    late_term = adj_two * (fwd_three - 2.0 * fwd_two + recent_own)
    early_term = adj_one * (fwd_two - 2.0 * recent_own + older)
    gradient = shot_sum(early_term + late_term)
    return (fwd_three[None], adj_one[None], gradient)


def solution(mesh):
    return jax.shard_map(
        shards,
        mesh=mesh,
        in_specs=(
            P("dom", None, None),
            P("shot", "dom", None, None),
            P("shot", "dom", None, None),
            P("shot", "dom", None, None),
            P("shot", "dom", None, None),
            P("shot"),
            P("shot"),
            P("shot"),
            P("shot", None),
            P("shot", None),
            P("shot", None),
            P("shot", None),
            P("shot", None, None),
        ),
        out_specs=(
            P("shot", "dom", None, None),
            P("shot", "dom", None, None),
            P("dom", None, None),
        ),
        check_vma=False,
    )
```

```python
import jax
import jax.numpy as jnp
from jax import lax
from jax.sharding import PartitionSpec as P

R = 4


stencil_weights = (-205.0 / 72.0, 8.0 / 5.0, -1.0 / 5.0, 8.0 / 315.0, -1.0 / 560.0)


def with_halo(block, sides, width):
    for axis, dim in sides:
        count = lax.axis_size(axis)
        forward = [(i, i + 1) for i in range(count - 1)]
        backward = [(target, source) for source, target in forward]
        low = lax.ppermute(
            lax.slice_in_dim(block, block.shape[dim] - width, None, axis=dim), axis, forward
        )
        high = lax.ppermute(lax.slice_in_dim(block, 0, width, axis=dim), axis, backward)
        block = jnp.concatenate([low, block, high], axis=dim)
    return block


def wide_halo(fields, widths):
    count = lax.axis_size("dom")
    forward = [(i, i + 1) for i in range(count - 1)]
    backward = [(target, source) for source, target in forward]
    tails = jnp.concatenate([f[f.shape[0] - w :] for f, w in zip(fields, widths)])
    heads = jnp.concatenate([f[:w] for f, w in zip(fields, widths)])
    lows = lax.ppermute(tails, "dom", forward)
    highs = lax.ppermute(heads, "dom", backward)
    out, at = [], 0
    for f, w in zip(fields, widths):
        out.append(jnp.concatenate([lows[at : at + w], f, highs[at : at + w]]))
        at += w
    return out


def laplace_core(extended):
    count = extended.shape[0] - 2 * R
    center = extended[R : R + count]
    width_y = center.shape[1]
    width_z = center.shape[2]
    total = 3.0 * stencil_weights[0] * center
    padded = jnp.pad(center, ((0, 0), (R, R), (R, R)))
    for offset in range(1, R + 1):
        weight = stencil_weights[offset]
        total = total + weight * (
            extended[R + offset : R + offset + count] + extended[R - offset : R - offset + count]
        )
        total = total + weight * (
            padded[:, R + offset : R + offset + width_y, R : R + width_z]
            + padded[:, R - offset : R - offset + width_y, R : R + width_z]
        )
        total = total + weight * (
            padded[:, R : R + width_y, R + offset : R + offset + width_z]
            + padded[:, R : R + width_y, R - offset : R - offset + width_z]
        )
    return total


def point_grid(shape, xcells, ycells, zcells, values, start):
    count = shape[0]
    inside = (xcells >= start) & (xcells < start + count)
    local = jnp.clip(xcells - start, 0, count - 1)
    kept = jnp.where(inside, values, jnp.zeros_like(values))
    return jnp.zeros(shape, values.dtype).at[local, ycells, zcells].add(kept)


def selectors(shape, xcells, ycells, zcells, start):
    width_x, width_y, width_z = shape
    inside = (xcells >= start) & (xcells < start + width_x)
    row = jnp.where(inside, (xcells - start) * width_y + ycells, -1)
    count = xcells.shape[0]
    rows = (row[:, None] == lax.broadcasted_iota(jnp.int32, (count, width_x * width_y), 1)).astype(jnp.float32)
    cols = (zcells[:, None] == lax.broadcasted_iota(jnp.int32, (count, width_z), 1)).astype(jnp.float32)
    return rows, cols


def sample(fields, rows, cols):
    width_x, width_y, width_z = fields[0].shape
    flat = jnp.concatenate([f.reshape(width_x * width_y, width_z) for f in fields], axis=1)
    picked = jnp.dot(rows, flat, precision=lax.Precision.HIGH)
    return [
        jnp.sum(picked[:, k * width_z : (k + 1) * width_z] * cols, axis=1)
        for k in range(len(fields))
    ]


def receiver_grid(shape, rows, cols, values):
    placed = lax.dot_general(
        rows * values[:, None], cols, (((0,), (0,)), ((), ())), precision=lax.Precision.HIGH
    )
    return placed.reshape(shape)


def shot_sum(term):
    count = lax.axis_size("shot")
    pieces = term.reshape((count, term.shape[0] // count) + term.shape[1:])
    mine = jnp.sum(lax.all_to_all(pieces, "shot", 0, 0, tiled=False), axis=0)
    spread = jnp.broadcast_to(mine[None], (count,) + mine.shape)
    return lax.all_to_all(spread, "shot", 0, 0, tiled=False).reshape(term.shape)


def shards(
    coefficient,
    fwd_older,
    fwd_recent,
    adj_later,
    adj_recent,
    source_xcell,
    source_ycell,
    source_zcell,
    amplitude,
    receiver_xcell,
    receiver_ycell,
    receiver_zcell,
    observed,
):
    count = coefficient.shape[0]
    shape = coefficient.shape
    base = lax.axis_index("dom") * count
    older = fwd_older[0]
    recent = fwd_recent[0]
    later = adj_later[0]
    adj_now = adj_recent[0]
    rxc = receiver_xcell[0]
    ryc = receiver_ycell[0]
    rzc = receiver_zcell[0]

    widths = (2 * R, R, R, R)
    fields = (recent, older, coefficient, adj_now)
    recent_x, older_x, coef_x, adj_now_x = wide_halo(fields, widths)

    def advance(current, before, coef, sources):
        return 2.0 * current[R:-R] - before + coef * (laplace_core(current) + sources)

    def source_grid(margin, step):
        return point_grid(
            (count + 2 * margin,) + shape[1:], source_xcell, source_ycell, source_zcell,
            amplitude[0, step : step + 1], base - margin,
        )

    fwd_two_x = advance(recent_x, older_x, coef_x, source_grid(R, 0))
    fwd_two = fwd_two_x[R:-R]
    recent_own = recent_x[2 * R : -2 * R]
    fwd_three = advance(fwd_two_x, recent_own, coefficient, source_grid(0, 1))
    rows, cols = selectors(shape, rxc, ryc, rzc, base)
    at_two, at_three = sample((fwd_two, fwd_three), rows, cols)
    resid_two = at_two - observed[0, 0]
    resid_three = at_three - observed[0, 1]
    adj_two = advance(adj_now_x, later, coefficient, receiver_grid(shape, rows, cols, resid_three))
    adj_one = advance(
        with_halo(adj_two, (("dom", 0),), R), adj_now, coefficient,
        receiver_grid(shape, rows, cols, resid_two),
    )
    late_term = adj_two * (fwd_three - 2.0 * fwd_two + recent_own)
    early_term = adj_one * (fwd_two - 2.0 * recent_own + older)
    gradient = shot_sum(early_term + late_term)
    return (fwd_three[None], adj_one[None], gradient)


def solution(mesh):
    return jax.shard_map(
        shards,
        mesh=mesh,
        in_specs=(
            P("dom", None, None),
            P("shot", "dom", None, None),
            P("shot", "dom", None, None),
            P("shot", "dom", None, None),
            P("shot", "dom", None, None),
            P("shot"),
            P("shot"),
            P("shot"),
            P("shot", None),
            P("shot", None),
            P("shot", None),
            P("shot", None),
            P("shot", None, None),
        ),
        out_specs=(
            P("shot", "dom", None, None),
            P("shot", "dom", None, None),
            P("dom", None, None),
        ),
        check_vma=False,
    )
```

```python
import jax
import jax.numpy as jnp
from jax import lax
from jax.sharding import PartitionSpec as P

R = 4


stencil_weights = (-205.0 / 72.0, 8.0 / 5.0, -1.0 / 5.0, 8.0 / 315.0, -1.0 / 560.0)


def with_halo(block, sides, width):
    for axis, dim in sides:
        count = lax.axis_size(axis)
        forward = [(i, i + 1) for i in range(count - 1)]
        backward = [(target, source) for source, target in forward]
        low = lax.ppermute(
            lax.slice_in_dim(block, block.shape[dim] - width, None, axis=dim), axis, forward
        )
        high = lax.ppermute(lax.slice_in_dim(block, 0, width, axis=dim), axis, backward)
        block = jnp.concatenate([low, block, high], axis=dim)
    return block


def wide_halo(fields, widths):
    count = lax.axis_size("dom")
    forward = [(i, i + 1) for i in range(count - 1)]
    backward = [(target, source) for source, target in forward]
    tails = jnp.concatenate([f[f.shape[0] - w :] for f, w in zip(fields, widths)])
    heads = jnp.concatenate([f[:w] for f, w in zip(fields, widths)])
    lows = lax.ppermute(tails, "dom", forward)
    highs = lax.ppermute(heads, "dom", backward)
    out, at = [], 0
    for f, w in zip(fields, widths):
        out.append(jnp.concatenate([lows[at : at + w], f, highs[at : at + w]]))
        at += w
    return out


def laplace_core(extended):
    count = extended.shape[0] - 2 * R
    center = extended[R : R + count]
    width_y = center.shape[1]
    width_z = center.shape[2]
    total = 3.0 * stencil_weights[0] * center
    padded = jnp.pad(center, ((0, 0), (R, R), (0, 0)))
    for offset in range(1, R + 1):
        weight = stencil_weights[offset]
        total = total + weight * (
            extended[R + offset : R + offset + count] + extended[R - offset : R - offset + count]
        )
        total = total + weight * (
            padded[:, R + offset : R + offset + width_y]
            + padded[:, R - offset : R - offset + width_y]
        )
    apart = lax.broadcasted_iota(jnp.int32, (width_z, width_z), 0) - lax.broadcasted_iota(
        jnp.int32, (width_z, width_z), 1
    )
    band = jnp.zeros((width_z, width_z), jnp.float32)
    for offset in range(1, R + 1):
        band = jnp.where(jnp.abs(apart) == offset, stencil_weights[offset], band)
    along_z = jnp.dot(
        center.reshape(count * width_y, width_z), band, precision=lax.Precision.HIGHEST
    )
    return total + along_z.reshape(center.shape)


def point_grid(shape, xcells, ycells, zcells, values, start):
    count = shape[0]
    inside = (xcells >= start) & (xcells < start + count)
    local = jnp.clip(xcells - start, 0, count - 1)
    kept = jnp.where(inside, values, jnp.zeros_like(values))
    return jnp.zeros(shape, values.dtype).at[local, ycells, zcells].add(kept)


def selectors(shape, xcells, ycells, zcells, start):
    width_x, width_y, width_z = shape
    inside = (xcells >= start) & (xcells < start + width_x)
    row = jnp.where(inside, (xcells - start) * width_y + ycells, -1)
    count = xcells.shape[0]
    rows = (row[:, None] == lax.broadcasted_iota(jnp.int32, (count, width_x * width_y), 1)).astype(jnp.float32)
    cols = (zcells[:, None] == lax.broadcasted_iota(jnp.int32, (count, width_z), 1)).astype(jnp.float32)
    return rows, cols


def sample(field, rows, cols):
    width_x, width_y, width_z = field.shape
    picked = jnp.dot(rows, field.reshape(width_x * width_y, width_z), precision=lax.Precision.HIGH)
    return jnp.sum(picked * cols, axis=1)


def receiver_grid(shape, rows, cols, values):
    placed = lax.dot_general(
        rows * values[:, None], cols, (((0,), (0,)), ((), ())), precision=lax.Precision.HIGH
    )
    return placed.reshape(shape)


def shot_sum(term):
    count = lax.axis_size("shot")
    pieces = term.reshape((count, term.shape[0] // count) + term.shape[1:])
    mine = jnp.sum(lax.all_to_all(pieces, "shot", 0, 0, tiled=False), axis=0)
    spread = jnp.broadcast_to(mine[None], (count,) + mine.shape)
    return lax.all_to_all(spread, "shot", 0, 0, tiled=False).reshape(term.shape)


def shards(
    coefficient,
    fwd_older,
    fwd_recent,
    adj_later,
    adj_recent,
    source_xcell,
    source_ycell,
    source_zcell,
    amplitude,
    receiver_xcell,
    receiver_ycell,
    receiver_zcell,
    observed,
):
    count = coefficient.shape[0]
    shape = coefficient.shape
    base = lax.axis_index("dom") * count
    older = fwd_older[0]
    recent = fwd_recent[0]
    later = adj_later[0]
    adj_now = adj_recent[0]
    rxc = receiver_xcell[0]
    ryc = receiver_ycell[0]
    rzc = receiver_zcell[0]

    widths = (2 * R, R, R, R)
    fields = (recent, older, coefficient, adj_now)
    recent_x, older_x, coef_x, adj_now_x = wide_halo(fields, widths)

    def advance(current, before, coef, sources):
        return 2.0 * current[R:-R] - before + coef * (laplace_core(current) + sources)

    def source_grid(margin, step):
        return point_grid(
            (count + 2 * margin,) + shape[1:], source_xcell, source_ycell, source_zcell,
            amplitude[0, step : step + 1], base - margin,
        )

    fwd_two_x = advance(recent_x, older_x, coef_x, source_grid(R, 0))
    fwd_two = fwd_two_x[R:-R]
    recent_own = recent_x[2 * R : -2 * R]
    fwd_three = advance(fwd_two_x, recent_own, coefficient, source_grid(0, 1))
    rows, cols = selectors(shape, rxc, ryc, rzc, base)
    resid_two = sample(fwd_two, rows, cols) - observed[0, 0]
    resid_three = sample(fwd_three, rows, cols) - observed[0, 1]
    adj_two = advance(adj_now_x, later, coefficient, receiver_grid(shape, rows, cols, resid_three))
    adj_one = advance(
        with_halo(adj_two, (("dom", 0),), R), adj_now, coefficient,
        receiver_grid(shape, rows, cols, resid_two),
    )
    late_term = adj_two * (fwd_three - 2.0 * fwd_two + recent_own)
    early_term = adj_one * (fwd_two - 2.0 * recent_own + older)
    gradient = shot_sum(early_term + late_term)
    return (fwd_three[None], adj_one[None], gradient)


def solution(mesh):
    return jax.shard_map(
        shards,
        mesh=mesh,
        in_specs=(
            P("dom", None, None),
            P("shot", "dom", None, None),
            P("shot", "dom", None, None),
            P("shot", "dom", None, None),
            P("shot", "dom", None, None),
            P("shot"),
            P("shot"),
            P("shot"),
            P("shot", None),
            P("shot", None),
            P("shot", None),
            P("shot", None),
            P("shot", None, None),
        ),
        out_specs=(
            P("shot", "dom", None, None),
            P("shot", "dom", None, None),
            P("dom", None, None),
        ),
        check_vma=False,
    )
```

```python
import jax
import jax.numpy as jnp
from jax import lax
from jax.sharding import PartitionSpec as P

R = 4


stencil_weights = (-205.0 / 72.0, 8.0 / 5.0, -1.0 / 5.0, 8.0 / 315.0, -1.0 / 560.0)


def with_halo(block, sides, width):
    for axis, dim in sides:
        count = lax.axis_size(axis)
        forward = [(i, i + 1) for i in range(count - 1)]
        backward = [(target, source) for source, target in forward]
        low = lax.ppermute(
            lax.slice_in_dim(block, block.shape[dim] - width, None, axis=dim), axis, forward
        )
        high = lax.ppermute(lax.slice_in_dim(block, 0, width, axis=dim), axis, backward)
        block = jnp.concatenate([low, block, high], axis=dim)
    return block


def wide_halo(fields, widths):
    count = lax.axis_size("dom")
    forward = [(i, i + 1) for i in range(count - 1)]
    backward = [(target, source) for source, target in forward]
    tails = jnp.concatenate([f[f.shape[0] - w :] for f, w in zip(fields, widths)])
    heads = jnp.concatenate([f[:w] for f, w in zip(fields, widths)])
    lows = lax.ppermute(tails, "dom", forward)
    highs = lax.ppermute(heads, "dom", backward)
    out, at = [], 0
    for f, w in zip(fields, widths):
        out.append(jnp.concatenate([lows[at : at + w], f, highs[at : at + w]]))
        at += w
    return out


def laplace_core(extended):
    count = extended.shape[0] - 2 * R
    center = extended[R : R + count]
    width_y = center.shape[1]
    width_z = center.shape[2]
    total = 3.0 * stencil_weights[0] * center
    padded = jnp.pad(center, ((0, 0), (R, R), (R, R)))
    for offset in range(1, R + 1):
        weight = stencil_weights[offset]
        total = total + weight * (
            extended[R + offset : R + offset + count] + extended[R - offset : R - offset + count]
        )
        total = total + weight * (
            padded[:, R + offset : R + offset + width_y, R : R + width_z]
            + padded[:, R - offset : R - offset + width_y, R : R + width_z]
        )
        total = total + weight * (
            padded[:, R : R + width_y, R + offset : R + offset + width_z]
            + padded[:, R : R + width_y, R - offset : R - offset + width_z]
        )
    return total


def laplace_banded(extended):
    count = extended.shape[0] - 2 * R
    center = extended[R : R + count]
    width_y = center.shape[1]
    width_z = center.shape[2]
    total = 3.0 * stencil_weights[0] * center
    padded = jnp.pad(center, ((0, 0), (R, R), (0, 0)))
    for offset in range(1, R + 1):
        weight = stencil_weights[offset]
        total = total + weight * (
            extended[R + offset : R + offset + count] + extended[R - offset : R - offset + count]
        )
        total = total + weight * (
            padded[:, R + offset : R + offset + width_y]
            + padded[:, R - offset : R - offset + width_y]
        )
    apart = lax.broadcasted_iota(jnp.int32, (width_z, width_z), 0) - lax.broadcasted_iota(
        jnp.int32, (width_z, width_z), 1
    )
    band = jnp.zeros((width_z, width_z), jnp.float32)
    for offset in range(1, R + 1):
        band = jnp.where(jnp.abs(apart) == offset, stencil_weights[offset], band)
    along_z = jnp.dot(
        center.reshape(count * width_y, width_z), band, precision=lax.Precision.HIGHEST
    )
    return total + along_z.reshape(center.shape)


def point_grid(shape, xcells, ycells, zcells, values, start):
    count = shape[0]
    inside = (xcells >= start) & (xcells < start + count)
    local = jnp.clip(xcells - start, 0, count - 1)
    kept = jnp.where(inside, values, jnp.zeros_like(values))
    return jnp.zeros(shape, values.dtype).at[local, ycells, zcells].add(kept)


def selectors(shape, xcells, ycells, zcells, start):
    width_x, width_y, width_z = shape
    inside = (xcells >= start) & (xcells < start + width_x)
    row = jnp.where(inside, (xcells - start) * width_y + ycells, -1)
    count = xcells.shape[0]
    rows = (row[:, None] == lax.broadcasted_iota(jnp.int32, (count, width_x * width_y), 1)).astype(jnp.float32)
    cols = (zcells[:, None] == lax.broadcasted_iota(jnp.int32, (count, width_z), 1)).astype(jnp.float32)
    return rows, cols


def sample(field, rows, cols):
    width_x, width_y, width_z = field.shape
    picked = jnp.dot(rows, field.reshape(width_x * width_y, width_z), precision=lax.Precision.HIGH)
    return jnp.sum(picked * cols, axis=1)


def receiver_grid(shape, rows, cols, values):
    placed = lax.dot_general(
        rows * values[:, None], cols, (((0,), (0,)), ((), ())), precision=lax.Precision.HIGH
    )
    return placed.reshape(shape)


def shot_sum(term):
    count = lax.axis_size("shot")
    pieces = term.reshape((count, term.shape[0] // count) + term.shape[1:])
    mine = jnp.sum(lax.all_to_all(pieces, "shot", 0, 0, tiled=False), axis=0)
    spread = jnp.broadcast_to(mine[None], (count,) + mine.shape)
    return lax.all_to_all(spread, "shot", 0, 0, tiled=False).reshape(term.shape)


def shards(
    coefficient,
    fwd_older,
    fwd_recent,
    adj_later,
    adj_recent,
    source_xcell,
    source_ycell,
    source_zcell,
    amplitude,
    receiver_xcell,
    receiver_ycell,
    receiver_zcell,
    observed,
):
    count = coefficient.shape[0]
    shape = coefficient.shape
    base = lax.axis_index("dom") * count
    older = fwd_older[0]
    recent = fwd_recent[0]
    later = adj_later[0]
    adj_now = adj_recent[0]
    rxc = receiver_xcell[0]
    ryc = receiver_ycell[0]
    rzc = receiver_zcell[0]

    widths = (2 * R, R, R, R)
    fields = (recent, older, coefficient, adj_now)
    recent_x, older_x, coef_x, adj_now_x = wide_halo(fields, widths)

    def advance(current, before, coef, sources, laplace=laplace_core):
        return 2.0 * current[R:-R] - before + coef * (laplace(current) + sources)

    def source_grid(margin, step):
        return point_grid(
            (count + 2 * margin,) + shape[1:], source_xcell, source_ycell, source_zcell,
            amplitude[0, step : step + 1], base - margin,
        )

    fwd_two_x = advance(recent_x, older_x, coef_x, source_grid(R, 0))
    fwd_two = fwd_two_x[R:-R]
    recent_own = recent_x[2 * R : -2 * R]
    fwd_three = advance(fwd_two_x, recent_own, coefficient, source_grid(0, 1))
    rows, cols = selectors(shape, rxc, ryc, rzc, base)
    resid_two = sample(fwd_two, rows, cols) - observed[0, 0]
    resid_three = sample(fwd_three, rows, cols) - observed[0, 1]
    adj_two = advance(
        adj_now_x, later, coefficient, receiver_grid(shape, rows, cols, resid_three), laplace_banded
    )
    adj_one = advance(
        with_halo(adj_two, (("dom", 0),), R), adj_now, coefficient,
        receiver_grid(shape, rows, cols, resid_two), laplace_banded,
    )
    late_term = adj_two * (fwd_three - 2.0 * fwd_two + recent_own)
    early_term = adj_one * (fwd_two - 2.0 * recent_own + older)
    gradient = shot_sum(early_term + late_term)
    return (fwd_three[None], adj_one[None], gradient)


def solution(mesh):
    return jax.shard_map(
        shards,
        mesh=mesh,
        in_specs=(
            P("dom", None, None),
            P("shot", "dom", None, None),
            P("shot", "dom", None, None),
            P("shot", "dom", None, None),
            P("shot", "dom", None, None),
            P("shot"),
            P("shot"),
            P("shot"),
            P("shot", None),
            P("shot", None),
            P("shot", None),
            P("shot", None),
            P("shot", None, None),
        ),
        out_specs=(
            P("shot", "dom", None, None),
            P("shot", "dom", None, None),
            P("dom", None, None),
        ),
        check_vma=False,
    )
```

```python
import jax
import jax.numpy as jnp
from jax import lax
from jax.sharding import PartitionSpec as P

R = 4


stencil_weights = (-205.0 / 72.0, 8.0 / 5.0, -1.0 / 5.0, 8.0 / 315.0, -1.0 / 560.0)


def with_halo(block, sides, width):
    for axis, dim in sides:
        count = lax.axis_size(axis)
        forward = [(i, i + 1) for i in range(count - 1)]
        backward = [(target, source) for source, target in forward]
        low = lax.ppermute(
            lax.slice_in_dim(block, block.shape[dim] - width, None, axis=dim), axis, forward
        )
        high = lax.ppermute(lax.slice_in_dim(block, 0, width, axis=dim), axis, backward)
        block = jnp.concatenate([low, block, high], axis=dim)
    return block


def wide_halo(fields, widths):
    count = lax.axis_size("dom")
    forward = [(i, i + 1) for i in range(count - 1)]
    backward = [(target, source) for source, target in forward]
    tails = jnp.concatenate([f[f.shape[0] - w :] for f, w in zip(fields, widths)])
    heads = jnp.concatenate([f[:w] for f, w in zip(fields, widths)])
    lows = lax.ppermute(tails, "dom", forward)
    highs = lax.ppermute(heads, "dom", backward)
    out, at = [], 0
    for f, w in zip(fields, widths):
        out.append(jnp.concatenate([lows[at : at + w], f, highs[at : at + w]]))
        at += w
    return out


def laplace_core(extended):
    count = extended.shape[0] - 2 * R
    center = extended[R : R + count]
    width_y = center.shape[1]
    width_z = center.shape[2]
    total = 3.0 * stencil_weights[0] * center
    padded = jnp.pad(center, ((0, 0), (R, R), (R, R)))
    for offset in range(1, R + 1):
        weight = stencil_weights[offset]
        total = total + weight * (
            extended[R + offset : R + offset + count] + extended[R - offset : R - offset + count]
        )
        total = total + weight * (
            padded[:, R + offset : R + offset + width_y, R : R + width_z]
            + padded[:, R - offset : R - offset + width_y, R : R + width_z]
        )
        total = total + weight * (
            padded[:, R : R + width_y, R + offset : R + offset + width_z]
            + padded[:, R : R + width_y, R - offset : R - offset + width_z]
        )
    return total


def point_grid(shape, xcells, ycells, zcells, values, start):
    count = shape[0]
    inside = (xcells >= start) & (xcells < start + count)
    local = jnp.clip(xcells - start, 0, count - 1)
    kept = jnp.where(inside, values, jnp.zeros_like(values))
    return jnp.zeros(shape, values.dtype).at[local, ycells, zcells].add(kept)


def selectors(shape, xcells, ycells, zcells, start):
    width_x, width_y, width_z = shape
    inside = (xcells >= start) & (xcells < start + width_x)
    row = jnp.where(inside, (xcells - start) * width_y + ycells, -1)
    count = xcells.shape[0]
    rows = (row[:, None] == lax.broadcasted_iota(jnp.int32, (count, width_x * width_y), 1)).astype(jnp.float32)
    cols = (zcells[:, None] == lax.broadcasted_iota(jnp.int32, (count, width_z), 1)).astype(jnp.float32)
    return rows, cols


def sample(field, rows, cols):
    width_x, width_y, width_z = field.shape
    picked = jnp.dot(rows, field.reshape(width_x * width_y, width_z), precision=lax.Precision.HIGH)
    return jnp.sum(picked * cols, axis=1)


def receiver_grid(shape, rows, cols, values):
    high = values.astype(jnp.bfloat16)
    rest = (values - high.astype(jnp.float32)).astype(jnp.bfloat16)
    picks = rows.astype(jnp.bfloat16)
    lhs = jnp.concatenate([picks * high[:, None], picks * rest[:, None]])
    rhs = jnp.concatenate([cols, cols]).astype(jnp.bfloat16)
    placed = lax.dot_general(
        lhs, rhs, (((0,), (0,)), ((), ())), preferred_element_type=jnp.float32
    )
    return placed.reshape(shape)


def shot_sum(term):
    count = lax.axis_size("shot")
    pieces = term.reshape((count, term.shape[0] // count) + term.shape[1:])
    mine = jnp.sum(lax.all_to_all(pieces, "shot", 0, 0, tiled=False), axis=0)
    spread = jnp.broadcast_to(mine[None], (count,) + mine.shape)
    return lax.all_to_all(spread, "shot", 0, 0, tiled=False).reshape(term.shape)


def shards(
    coefficient,
    fwd_older,
    fwd_recent,
    adj_later,
    adj_recent,
    source_xcell,
    source_ycell,
    source_zcell,
    amplitude,
    receiver_xcell,
    receiver_ycell,
    receiver_zcell,
    observed,
):
    count = coefficient.shape[0]
    shape = coefficient.shape
    base = lax.axis_index("dom") * count
    older = fwd_older[0]
    recent = fwd_recent[0]
    later = adj_later[0]
    adj_now = adj_recent[0]
    rxc = receiver_xcell[0]
    ryc = receiver_ycell[0]
    rzc = receiver_zcell[0]

    widths = (2 * R, R, R, R)
    fields = (recent, older, coefficient, adj_now)
    recent_x, older_x, coef_x, adj_now_x = wide_halo(fields, widths)

    def advance(current, before, coef, sources):
        return 2.0 * current[R:-R] - before + coef * (laplace_core(current) + sources)

    def source_grid(margin, step):
        return point_grid(
            (count + 2 * margin,) + shape[1:], source_xcell, source_ycell, source_zcell,
            amplitude[0, step : step + 1], base - margin,
        )

    fwd_two_x = advance(recent_x, older_x, coef_x, source_grid(R, 0))
    fwd_two = fwd_two_x[R:-R]
    recent_own = recent_x[2 * R : -2 * R]
    fwd_three = advance(fwd_two_x, recent_own, coefficient, source_grid(0, 1))
    rows, cols = selectors(shape, rxc, ryc, rzc, base)
    resid_two = sample(fwd_two, rows, cols) - observed[0, 0]
    resid_three = sample(fwd_three, rows, cols) - observed[0, 1]
    adj_two = advance(adj_now_x, later, coefficient, receiver_grid(shape, rows, cols, resid_three))
    adj_one = advance(
        with_halo(adj_two, (("dom", 0),), R), adj_now, coefficient,
        receiver_grid(shape, rows, cols, resid_two),
    )
    late_term = adj_two * (fwd_three - 2.0 * fwd_two + recent_own)
    early_term = adj_one * (fwd_two - 2.0 * recent_own + older)
    gradient = shot_sum(early_term + late_term)
    return (fwd_three[None], adj_one[None], gradient)


def solution(mesh):
    return jax.shard_map(
        shards,
        mesh=mesh,
        in_specs=(
            P("dom", None, None),
            P("shot", "dom", None, None),
            P("shot", "dom", None, None),
            P("shot", "dom", None, None),
            P("shot", "dom", None, None),
            P("shot"),
            P("shot"),
            P("shot"),
            P("shot", None),
            P("shot", None),
            P("shot", None),
            P("shot", None),
            P("shot", None, None),
        ),
        out_specs=(
            P("shot", "dom", None, None),
            P("shot", "dom", None, None),
            P("dom", None, None),
        ),
        check_vma=False,
    )
```

```python
import jax
import jax.numpy as jnp
from jax import lax
from jax.sharding import PartitionSpec as P

R = 4


stencil_weights = (-205.0 / 72.0, 8.0 / 5.0, -1.0 / 5.0, 8.0 / 315.0, -1.0 / 560.0)


def with_halo(block, sides, width):
    for axis, dim in sides:
        count = lax.axis_size(axis)
        forward = [(i, i + 1) for i in range(count - 1)]
        backward = [(target, source) for source, target in forward]
        low = lax.ppermute(
            lax.slice_in_dim(block, block.shape[dim] - width, None, axis=dim), axis, forward
        )
        high = lax.ppermute(lax.slice_in_dim(block, 0, width, axis=dim), axis, backward)
        block = jnp.concatenate([low, block, high], axis=dim)
    return block


def wide_halo(fields, widths):
    count = lax.axis_size("dom")
    forward = [(i, i + 1) for i in range(count - 1)]
    backward = [(target, source) for source, target in forward]
    tails = jnp.concatenate([f[f.shape[0] - w :] for f, w in zip(fields, widths)])
    heads = jnp.concatenate([f[:w] for f, w in zip(fields, widths)])
    lows = lax.ppermute(tails, "dom", forward)
    highs = lax.ppermute(heads, "dom", backward)
    out, at = [], 0
    for f, w in zip(fields, widths):
        out.append(jnp.concatenate([lows[at : at + w], f, highs[at : at + w]]))
        at += w
    return out


def laplace_core(extended):
    count = extended.shape[0] - 2 * R
    center = extended[R : R + count]
    width_y = center.shape[1]
    width_z = center.shape[2]
    total = 3.0 * stencil_weights[0] * center
    padded = jnp.pad(center, ((0, 0), (R, R), (R, R)))
    for offset in range(1, R + 1):
        weight = stencil_weights[offset]
        total = total + weight * (
            extended[R + offset : R + offset + count] + extended[R - offset : R - offset + count]
        )
        total = total + weight * (
            padded[:, R + offset : R + offset + width_y, R : R + width_z]
            + padded[:, R - offset : R - offset + width_y, R : R + width_z]
        )
        total = total + weight * (
            padded[:, R : R + width_y, R + offset : R + offset + width_z]
            + padded[:, R : R + width_y, R - offset : R - offset + width_z]
        )
    return total


def point_grid(shape, xcells, ycells, zcells, values, start):
    count = shape[0]
    inside = (xcells >= start) & (xcells < start + count)
    local = jnp.clip(xcells - start, 0, count - 1)
    kept = jnp.where(inside, values, jnp.zeros_like(values))
    return jnp.zeros(shape, values.dtype).at[local, ycells, zcells].add(kept)


def selectors(shape, xcells, ycells, zcells, start):
    width_x, width_y, width_z = shape
    inside = (xcells >= start) & (xcells < start + width_x)
    row = jnp.where(inside, (xcells - start) * width_y + ycells, -1)
    count = xcells.shape[0]
    rows = (row[:, None] == lax.broadcasted_iota(jnp.int32, (count, width_x * width_y), 1)).astype(jnp.float32)
    cols = (zcells[:, None] == lax.broadcasted_iota(jnp.int32, (count, width_z), 1)).astype(jnp.float32)
    return rows, cols


def sample(field, rows, cols):
    width_x, width_y, width_z = field.shape
    along = lax.dot_general(
        field.reshape(width_x * width_y, width_z), cols, (((1,), (1,)), ((), ())),
        precision=lax.Precision.HIGH,
    )
    return jnp.sum(along * rows.T, axis=0)


def receiver_grid(shape, rows, cols, values):
    placed = lax.dot_general(
        rows * values[:, None], cols, (((0,), (0,)), ((), ())), precision=lax.Precision.HIGH
    )
    return placed.reshape(shape)


def shot_sum(term):
    count = lax.axis_size("shot")
    pieces = term.reshape((count, term.shape[0] // count) + term.shape[1:])
    mine = jnp.sum(lax.all_to_all(pieces, "shot", 0, 0, tiled=False), axis=0)
    spread = jnp.broadcast_to(mine[None], (count,) + mine.shape)
    return lax.all_to_all(spread, "shot", 0, 0, tiled=False).reshape(term.shape)


def shards(
    coefficient,
    fwd_older,
    fwd_recent,
    adj_later,
    adj_recent,
    source_xcell,
    source_ycell,
    source_zcell,
    amplitude,
    receiver_xcell,
    receiver_ycell,
    receiver_zcell,
    observed,
):
    count = coefficient.shape[0]
    shape = coefficient.shape
    base = lax.axis_index("dom") * count
    older = fwd_older[0]
    recent = fwd_recent[0]
    later = adj_later[0]
    adj_now = adj_recent[0]
    rxc = receiver_xcell[0]
    ryc = receiver_ycell[0]
    rzc = receiver_zcell[0]

    widths = (2 * R, R, R, R)
    fields = (recent, older, coefficient, adj_now)
    recent_x, older_x, coef_x, adj_now_x = wide_halo(fields, widths)

    def advance(current, before, coef, sources):
        return 2.0 * current[R:-R] - before + coef * (laplace_core(current) + sources)

    def source_grid(margin, step):
        return point_grid(
            (count + 2 * margin,) + shape[1:], source_xcell, source_ycell, source_zcell,
            amplitude[0, step : step + 1], base - margin,
        )

    fwd_two_x = advance(recent_x, older_x, coef_x, source_grid(R, 0))
    fwd_two = fwd_two_x[R:-R]
    recent_own = recent_x[2 * R : -2 * R]
    fwd_three = advance(fwd_two_x, recent_own, coefficient, source_grid(0, 1))
    rows, cols = selectors(shape, rxc, ryc, rzc, base)
    resid_two = sample(fwd_two, rows, cols) - observed[0, 0]
    resid_three = sample(fwd_three, rows, cols) - observed[0, 1]
    adj_two = advance(adj_now_x, later, coefficient, receiver_grid(shape, rows, cols, resid_three))
    adj_one = advance(
        with_halo(adj_two, (("dom", 0),), R), adj_now, coefficient,
        receiver_grid(shape, rows, cols, resid_two),
    )
    late_term = adj_two * (fwd_three - 2.0 * fwd_two + recent_own)
    early_term = adj_one * (fwd_two - 2.0 * recent_own + older)
    gradient = shot_sum(early_term + late_term)
    return (fwd_three[None], adj_one[None], gradient)


def solution(mesh):
    return jax.shard_map(
        shards,
        mesh=mesh,
        in_specs=(
            P("dom", None, None),
            P("shot", "dom", None, None),
            P("shot", "dom", None, None),
            P("shot", "dom", None, None),
            P("shot", "dom", None, None),
            P("shot"),
            P("shot"),
            P("shot"),
            P("shot", None),
            P("shot", None),
            P("shot", None),
            P("shot", None),
            P("shot", None, None),
        ),
        out_specs=(
            P("shot", "dom", None, None),
            P("shot", "dom", None, None),
            P("dom", None, None),
        ),
        check_vma=False,
    )
```

```python
import jax
import jax.numpy as jnp
from jax import lax
from jax.sharding import PartitionSpec as P

R = 4


stencil_weights = (-205.0 / 72.0, 8.0 / 5.0, -1.0 / 5.0, 8.0 / 315.0, -1.0 / 560.0)


def with_halo(block, sides, width):
    for axis, dim in sides:
        count = lax.axis_size(axis)
        forward = [(i, i + 1) for i in range(count - 1)]
        backward = [(target, source) for source, target in forward]
        low = lax.ppermute(
            lax.slice_in_dim(block, block.shape[dim] - width, None, axis=dim), axis, forward
        )
        high = lax.ppermute(lax.slice_in_dim(block, 0, width, axis=dim), axis, backward)
        block = jnp.concatenate([low, block, high], axis=dim)
    return block


def wide_halo(fields, widths):
    count = lax.axis_size("dom")
    forward = [(i, i + 1) for i in range(count - 1)]
    backward = [(target, source) for source, target in forward]
    tails = jnp.concatenate([f[f.shape[0] - w :] for f, w in zip(fields, widths)])
    heads = jnp.concatenate([f[:w] for f, w in zip(fields, widths)])
    lows = lax.ppermute(tails, "dom", forward)
    highs = lax.ppermute(heads, "dom", backward)
    out, at = [], 0
    for f, w in zip(fields, widths):
        out.append(jnp.concatenate([lows[at : at + w], f, highs[at : at + w]]))
        at += w
    return out


def laplace_core(extended):
    count = extended.shape[0] - 2 * R
    center = extended[R : R + count]
    width_y = center.shape[1]
    width_z = center.shape[2]
    total = 3.0 * stencil_weights[0] * center
    padded = jnp.pad(center, ((0, 0), (R, R), (R, R)))
    for offset in range(1, R + 1):
        weight = stencil_weights[offset]
        total = total + weight * (
            extended[R + offset : R + offset + count] + extended[R - offset : R - offset + count]
        )
        total = total + weight * (
            padded[:, R + offset : R + offset + width_y, R : R + width_z]
            + padded[:, R - offset : R - offset + width_y, R : R + width_z]
        )
        total = total + weight * (
            padded[:, R : R + width_y, R + offset : R + offset + width_z]
            + padded[:, R : R + width_y, R - offset : R - offset + width_z]
        )
    return total


def point_grid(shape, xcells, ycells, zcells, values, start):
    count = shape[0]
    inside = (xcells >= start) & (xcells < start + count)
    local = jnp.clip(xcells - start, 0, count - 1)
    kept = jnp.where(inside, values, jnp.zeros_like(values))
    return jnp.zeros(shape, values.dtype).at[local, ycells, zcells].add(kept)


def selectors(shape, xcells, ycells, zcells, start):
    width_x, width_y, width_z = shape
    inside = (xcells >= start) & (xcells < start + width_x)
    row = jnp.where(inside, (xcells - start) * width_y + ycells, -1)
    count = xcells.shape[0]
    rows = (row[None, :] == lax.broadcasted_iota(jnp.int32, (width_x * width_y, count), 0)).astype(jnp.float32)
    cols = (zcells[:, None] == lax.broadcasted_iota(jnp.int32, (count, width_z), 1)).astype(jnp.float32)
    return rows, cols


def sample(field, rows, cols):
    width_x, width_y, width_z = field.shape
    along = lax.dot_general(
        field.reshape(width_x * width_y, width_z), cols, (((1,), (1,)), ((), ())),
        precision=lax.Precision.HIGH,
    )
    return jnp.sum(along * rows, axis=0)


def receiver_grid(shape, rows, cols, values):
    placed = lax.dot_general(
        rows * values[None, :], cols, (((1,), (0,)), ((), ())), precision=lax.Precision.HIGH
    )
    return placed.reshape(shape)


def shot_sum(term):
    count = lax.axis_size("shot")
    pieces = term.reshape((count, term.shape[0] // count) + term.shape[1:])
    mine = jnp.sum(lax.all_to_all(pieces, "shot", 0, 0, tiled=False), axis=0)
    spread = jnp.broadcast_to(mine[None], (count,) + mine.shape)
    return lax.all_to_all(spread, "shot", 0, 0, tiled=False).reshape(term.shape)


def shards(
    coefficient,
    fwd_older,
    fwd_recent,
    adj_later,
    adj_recent,
    source_xcell,
    source_ycell,
    source_zcell,
    amplitude,
    receiver_xcell,
    receiver_ycell,
    receiver_zcell,
    observed,
):
    count = coefficient.shape[0]
    shape = coefficient.shape
    base = lax.axis_index("dom") * count
    older = fwd_older[0]
    recent = fwd_recent[0]
    later = adj_later[0]
    adj_now = adj_recent[0]
    rxc = receiver_xcell[0]
    ryc = receiver_ycell[0]
    rzc = receiver_zcell[0]

    widths = (2 * R, R, R, R)
    fields = (recent, older, coefficient, adj_now)
    recent_x, older_x, coef_x, adj_now_x = wide_halo(fields, widths)

    def advance(current, before, coef, sources):
        return 2.0 * current[R:-R] - before + coef * (laplace_core(current) + sources)

    def source_grid(margin, step):
        return point_grid(
            (count + 2 * margin,) + shape[1:], source_xcell, source_ycell, source_zcell,
            amplitude[0, step : step + 1], base - margin,
        )

    fwd_two_x = advance(recent_x, older_x, coef_x, source_grid(R, 0))
    fwd_two = fwd_two_x[R:-R]
    recent_own = recent_x[2 * R : -2 * R]
    fwd_three = advance(fwd_two_x, recent_own, coefficient, source_grid(0, 1))
    rows, cols = selectors(shape, rxc, ryc, rzc, base)
    resid_two = sample(fwd_two, rows, cols) - observed[0, 0]
    resid_three = sample(fwd_three, rows, cols) - observed[0, 1]
    adj_two = advance(adj_now_x, later, coefficient, receiver_grid(shape, rows, cols, resid_three))
    adj_one = advance(
        with_halo(adj_two, (("dom", 0),), R), adj_now, coefficient,
        receiver_grid(shape, rows, cols, resid_two),
    )
    late_term = adj_two * (fwd_three - 2.0 * fwd_two + recent_own)
    early_term = adj_one * (fwd_two - 2.0 * recent_own + older)
    gradient = shot_sum(early_term + late_term)
    return (fwd_three[None], adj_one[None], gradient)


def solution(mesh):
    return jax.shard_map(
        shards,
        mesh=mesh,
        in_specs=(
            P("dom", None, None),
            P("shot", "dom", None, None),
            P("shot", "dom", None, None),
            P("shot", "dom", None, None),
            P("shot", "dom", None, None),
            P("shot"),
            P("shot"),
            P("shot"),
            P("shot", None),
            P("shot", None),
            P("shot", None),
            P("shot", None),
            P("shot", None, None),
        ),
        out_specs=(
            P("shot", "dom", None, None),
            P("shot", "dom", None, None),
            P("dom", None, None),
        ),
        check_vma=False,
    )
```
